128 devices in a mesh: dp: 8 (over z, core), fsdp: 16 (over x, y).
Axes of the slice: x: 4, y: 4, z: 4, core: 2. Of those that a mesh axis runs over, the one named last changes fastest.
Arguments:
- hidden: bfloat16 [98304, 8192], P(('dp', 'fsdp')), may hold values from -24 to 24
- head: bfloat16 [512, 8192], P('fsdp'), may hold values from -0.0625 to 0.0625
- labels: int32 [98304], P(('dp', 'fsdp')), may hold values from 0 to 511
- lse: float32 [98304], P(('dp', 'fsdp')), may hold values from 0 to 1.5
- cotangent: float32 [98304], P(('dp', 'fsdp')), may hold values from -0.6 to 0.6
- block_lists: int32 [768, 4], P(('dp', 'fsdp')), may hold values from -1 to 3, as said below
Outputs:
- grad_hidden: bfloat16 [98304, 8192], P(('dp', 'fsdp'))
- grad_head: bfloat16 [512, 8192], P('fsdp', 'dp')
The draws below stay inside these ranges and needn't reach their ends.
Inputs may be any that keep to these rules, and one draw needn't show every extreme that they name: `block_lists`: each row names distinct vocabulary blocks in its first slots (at least one) and -1 in the remaining slots.
All inputs are finite; a program needn't handle non-finite values.
Results may differ from the reference program's by a relative error of at most 0.0056.
Values may be sent and summed in bfloat16 or wider, within the bound.
No kernel may reach another device: no remote copies, remote signals or barrier semaphores. Data moves between devices by JAX's collectives and lax.ppermute only.
A program may use at most 192 MiB of HBM per device.

```python
import jax
import jax.numpy as jnp
from jax import lax

D = 8192
VB = 128
TB = 128
VBLOCKS = 4
T_DEV = 768
VOCAB = 512
TOKENS = 98304
NTB = 768


def draw_block_lists(key, part):
    blocks_all = TOKENS // TB
    groups = TOKENS // T_DEV
    per_group = T_DEV // TB
    key_level = jax.random.fold_in(key, 11)
    key_jitter = jax.random.fold_in(key, 23)
    key_order = jax.random.fold_in(key, 37)
    level = jax.random.randint(key_level, (groups,), 1, VBLOCKS + 1)
    level = jnp.repeat(level, per_group)
    jitter = jax.random.randint(key_jitter, (blocks_all,), -1, 2)
    count = jnp.clip(level + jitter, 1, VBLOCKS)
    scores = jax.random.randint(key_order, (blocks_all, VBLOCKS), 0, 1 << 20) * VBLOCKS + jnp.arange(VBLOCKS, dtype=jnp.int32)[None, :]
    order = jnp.argsort(scores, axis=1).astype(jnp.int32)
    slots = jnp.arange(VBLOCKS, dtype=jnp.int32)[None, :]
    return jnp.where(slots < count[:, None], order, -1).astype(jnp.int32)


def set_ends(values, rng, low, largest):
    dims = values.shape
    spot = [jax.random.randint(jax.random.fold_in(rng, axis), (), 0, dims[axis]) for axis in range(len(dims))]
    values = values.at[tuple(spot)].set(low)
    longest = dims.index(max(dims))
    spot[longest] = (spot[longest] + 1) % dims[longest]
    return values.at[tuple(spot)].set(largest)


def strengthened(array, key, source, target, shards_of, factor):
    owner, partner = [(jnp.arange(array.shape[dim]) // (array.shape[dim] // shards_of)).reshape([-1 if axis == dim else 1 for axis in range(array.ndim)]) for dim in (source, target)]
    chosen = jax.random.permutation(key, shards_of)[partner]
    strong = (owner == chosen) | (owner == (partner + shards_of // 2) % shards_of)
    return jnp.where(strong, factor * array, array)


def steps_of(own_key, shape, shards, low, high):
    gain, own = 1.0, jax.random.fold_in(own_key, 6)
    for position, shards_of in shards:
        draws = jnp.exp(jax.random.uniform(jax.random.fold_in(own, position), (shards_of,), jnp.float32, low / len(shards), high / len(shards)))
        gain = gain * jnp.repeat(draws, shape[position] // shards_of).reshape([-1 if axis == position else 1 for axis in range(len(shape))])
    return gain


def centred(stream_key, extent, width, reach, split=(), kind=jnp.bfloat16):
    entries = jax.random.normal(stream_key, extent, jnp.float32) * width
    if len(split) > 0:
        entries = steps_of(stream_key, extent, split, -0.22, 0.18) * entries
    return jnp.clip(entries, min=-reach, max=reach).astype(kind)


def bell_draw_with(key, extent, deviation, reach, pieces, heavy, held_as=jnp.bfloat16):
    result = deviation * jax.random.normal(key, extent, jnp.float32)
    if pieces:
        result = result * steps_of(key, extent, pieces, -0.22, 0.18)
    return jnp.clip(strengthened(result, jax.random.fold_in(key, 3), *heavy), -reach, reach).astype(held_as)


def setup_inputs(seed: int = 0) -> dict:
    seeds = jax.random.split(jax.random.key(seed), 7)
    hidden = bell_draw_with(seeds[0], (TOKENS, D), 1.0, 24.0, ((0, 128),), (0, 1, 128, 5.5))
    head = centred(seeds[1], (VOCAB, D), D ** -0.5, 0.0625, ((0, 16),))
    labels = set_ends(jax.random.randint(seeds[2], (TOKENS,), 0, VOCAB), jax.random.fold_in(seeds[2], 1), 0, VOCAB - 1).astype(jnp.int32)
    lse = jnp.clip(1.5 * jax.random.uniform(seeds[3], (TOKENS,), jnp.float32) ** steps_of(seeds[3], (TOKENS,), ((0, 128),), -0.2, 0.2), 0.0, 1.5)
    cotangent = centred(seeds[4], (TOKENS,), 0.1, 0.6, ((0, 128),), jnp.float32)
    block_lists = draw_block_lists(jax.random.fold_in(seeds[6], 71), 0)
    return {"hidden": hidden, "head": head, "labels": labels, "lse": lse, "cotangent": cotangent, "block_lists": block_lists}


def reference(hidden, head, labels, lse, cotangent, block_lists):
    listed = jnp.any(block_lists[:, :, None] == jnp.arange(VBLOCKS, dtype=jnp.int32)[None, None, :], axis=1)
    mask = jnp.repeat(listed, VB, axis=1).astype(jnp.float32)
    columns = jnp.arange(VB * VBLOCKS, dtype=jnp.int32)
    hidden_blocks = hidden.reshape(NTB, TB, D)
    label_blocks = labels.reshape(NTB, TB)
    lse_blocks = lse.reshape(NTB, TB)
    cot_blocks = cotangent.reshape(NTB, TB)

    def advance(total, items):
        rows, targets, norms, scales, keep = items
        logits = jnp.dot(rows, head.T, preferred_element_type=jnp.float32)
        hits = (targets[:, None] == columns[None, :]).astype(jnp.float32)
        grad_logits = (scales[:, None] * (keep[None, :] * jnp.exp(logits - norms[:, None]) - hits)).astype(jnp.bfloat16)
        grad_rows = jnp.dot(grad_logits, head, preferred_element_type=jnp.float32).astype(jnp.bfloat16)
        total = total + jnp.dot(grad_logits.T, rows, preferred_element_type=jnp.float32)
        return total, grad_rows

    start = jnp.zeros((VB * VBLOCKS, D), jnp.float32)
    total, grad_rows = lax.scan(advance, start, (hidden_blocks, label_blocks, lse_blocks, cot_blocks, mask))
    return grad_rows.reshape(NTB * TB, D), total.astype(jnp.bfloat16)
```

```python
import jax
import jax.numpy as jnp
from jax import lax
from jax.sharding import PartitionSpec as P

VB = 128
TB = 128
VBLOCKS = 4


def on_device(hidden, head, labels, lse, cotangent, block_lists):
    vocab = VB * VBLOCKS
    block_ids = jnp.arange(VBLOCKS, dtype=jnp.int32)
    listed = jnp.any(block_lists[:, :, None] == block_ids[None, None, :], axis=1)
    mask = jnp.repeat(jnp.repeat(listed, TB, axis=0), VB, axis=1).astype(jnp.float32)
    full_head = lax.all_gather(head, "fsdp", axis=0, tiled=True)
    logits = lax.dot_general(
        hidden, full_head, (((1,), (1,)), ((), ())), preferred_element_type=jnp.float32
    )
    columns = jnp.arange(vocab, dtype=jnp.int32)
    hits = (labels[:, None] == columns[None, :]).astype(jnp.float32)
    grad_logits = (
        cotangent[:, None] * (mask * jnp.exp(logits - lse[:, None]) - hits)
    ).astype(jnp.bfloat16)
    grad_hidden = jnp.dot(grad_logits, full_head, preferred_element_type=jnp.float32)
    term = lax.dot_general(
        grad_logits, hidden, (((0,), (0,)), ((), ())), preferred_element_type=jnp.float32
    )
    slab_part = lax.psum_scatter(term, "fsdp", scatter_dimension=0, tiled=True)
    owned = lax.psum_scatter(slab_part, "dp", scatter_dimension=1, tiled=True)
    return (grad_hidden.astype(jnp.bfloat16), owned.astype(jnp.bfloat16))


def solution(mesh):
    return jax.shard_map(
        on_device,
        mesh=mesh,
        in_specs=(
            P(("dp", "fsdp"), None),
            P("fsdp", None),
            P(("dp", "fsdp")),
            P(("dp", "fsdp")),
            P(("dp", "fsdp")),
            P(("dp", "fsdp"), None),
        ),
        out_specs=(P(("dp", "fsdp"), None), P("fsdp", "dp")),
        check_vma=False,
    )
```

```python
import jax
import jax.numpy as jnp
from jax import lax
from jax.sharding import PartitionSpec as P

VB = 128
TB = 128
VBLOCKS = 4


def on_device(hidden, head, labels, lse, cotangent, block_lists):
    vocab = VB * VBLOCKS
    dp = lax.axis_size("dp")
    width = hidden.shape[1]
    chunk = width // dp
    d = lax.axis_index("dp")
    core = d % 2
    zpos = d // 2
    rings = dp // 2
    block_ids = jnp.arange(VBLOCKS, dtype=jnp.int32)
    listed = jnp.any(block_lists[:, :, None] == block_ids[None, None, :], axis=1)
    mask = jnp.repeat(jnp.repeat(listed, TB, axis=0), VB, axis=1).astype(jnp.float32)
    full_head = lax.all_gather(head, "fsdp", axis=0, tiled=True)
    logits = lax.dot_general(
        hidden, full_head, (((1,), (1,)), ((), ())), preferred_element_type=jnp.float32
    )
    columns = jnp.arange(vocab, dtype=jnp.int32)
    hits = (labels[:, None] == columns[None, :]).astype(jnp.float32)
    grad_logits = (
        cotangent[:, None] * (mask * jnp.exp(logits - lse[:, None]) - hits)
    ).astype(jnp.bfloat16)
    split = hidden.reshape(hidden.shape[0], rings, 2, chunk)
    half = (hidden.shape[0], rings * chunk)
    keep_rows = lax.dynamic_index_in_dim(split, core, axis=2, keepdims=False).reshape(half)
    send_rows = lax.dynamic_index_in_dim(split, 1 - core, axis=2, keepdims=False).reshape(half)
    contract = (((0,), (0,)), ((), ()))
    parts = (vocab, rings, chunk)
    send = lax.dot_general(grad_logits, send_rows, contract, preferred_element_type=jnp.float32)
    keep = lax.dot_general(grad_logits, keep_rows, contract, preferred_element_type=jnp.float32)
    send = send.reshape(parts)
    keep = keep.reshape(parts)
    got = lax.ppermute(send, "dp", [(i, i ^ 1) for i in range(dp)])
    chip = keep + got
    grad_hidden = jnp.dot(grad_logits, full_head, preferred_element_type=jnp.float32)
    part = lax.psum_scatter(chip, "fsdp", scatter_dimension=0, tiled=True)
    ring = [(i, (i + 2) % dp) for i in range(dp)]
    acc = lax.dynamic_index_in_dim(part, (zpos - 1) % rings, axis=1, keepdims=False)
    for step in range(rings - 1):
        acc = lax.ppermute(acc, "dp", ring)
        acc = acc + lax.dynamic_index_in_dim(part, (zpos - 2 - step) % rings, axis=1, keepdims=False)
    return (grad_hidden.astype(jnp.bfloat16), acc.astype(jnp.bfloat16))


def solution(mesh):
    return jax.shard_map(
        on_device,
        mesh=mesh,
        in_specs=(
            P(("dp", "fsdp"), None),
            P("fsdp", None),
            P(("dp", "fsdp")),
            P(("dp", "fsdp")),
            P(("dp", "fsdp")),
            P(("dp", "fsdp"), None),
        ),
        out_specs=(P(("dp", "fsdp"), None), P("fsdp", "dp")),
        check_vma=False,
    )
```

```python
import jax
import jax.numpy as jnp
from jax import lax
from jax.sharding import PartitionSpec as P

VB = 128
TB = 128
VBLOCKS = 4


def on_device(hidden, head, labels, lse, cotangent, block_lists):
    vocab = VB * VBLOCKS
    dp = lax.axis_size("dp")
    width = hidden.shape[1]
    chunk = width // dp
    d = lax.axis_index("dp")
    core = d % 2
    zpos = d // 2
    rings = dp // 2
    block_ids = jnp.arange(VBLOCKS, dtype=jnp.int32)
    listed = jnp.any(block_lists[:, :, None] == block_ids[None, None, :], axis=1)
    mask = jnp.repeat(jnp.repeat(listed, TB, axis=0), VB, axis=1).astype(jnp.float32)
    full_head = lax.all_gather(head, "fsdp", axis=0, tiled=True)
    logits = lax.dot_general(
        hidden, full_head, (((1,), (1,)), ((), ())), preferred_element_type=jnp.float32
    )
    columns = jnp.arange(vocab, dtype=jnp.int32)
    hits = (labels[:, None] == columns[None, :]).astype(jnp.float32)
    grad_logits = (
        cotangent[:, None] * (mask * jnp.exp(logits - lse[:, None]) - hits)
    ).astype(jnp.bfloat16)
    def columns_of(parity):
        picks = [
            lax.dynamic_slice_in_dim(hidden, (2 * j + parity) * chunk, chunk, axis=1)
            for j in range(rings)
        ]
        return jnp.concatenate(picks, axis=1)

    contract = (((0,), (0,)), ((), ()))
    send = lax.dot_general(
        grad_logits, columns_of(1 - core), contract, preferred_element_type=jnp.float32
    )
    got = lax.ppermute(send, "dp", [(i, i ^ 1) for i in range(dp)])
    keep = lax.dot_general(
        grad_logits, columns_of(core), contract, preferred_element_type=jnp.float32
    )
    chip = keep + got
    grad_hidden = jnp.dot(grad_logits, full_head, preferred_element_type=jnp.float32)
    part = lax.psum_scatter(chip, "fsdp", scatter_dimension=0, tiled=True)
    ring = [(i, (i + 2) % dp) for i in range(dp)]
    acc = lax.dynamic_slice_in_dim(part, ((zpos - 1) % rings) * chunk, chunk, axis=1)
    for step in range(rings - 1):
        acc = lax.ppermute(acc, "dp", ring)
        own = lax.dynamic_slice_in_dim(part, ((zpos - 2 - step) % rings) * chunk, chunk, axis=1)
        acc = acc + own
    return (grad_hidden.astype(jnp.bfloat16), acc.astype(jnp.bfloat16))


def solution(mesh):
    return jax.shard_map(
        on_device,
        mesh=mesh,
        in_specs=(
            P(("dp", "fsdp"), None),
            P("fsdp", None),
            P(("dp", "fsdp")),
            P(("dp", "fsdp")),
            P(("dp", "fsdp")),
            P(("dp", "fsdp"), None),
        ),
        out_specs=(P(("dp", "fsdp"), None), P("fsdp", "dp")),
        check_vma=False,
    )
```

```python
import jax
import jax.numpy as jnp
from jax import lax
from jax.sharding import PartitionSpec as P

VB = 128
TB = 128
VBLOCKS = 4


def on_device(hidden, head, labels, lse, cotangent, block_lists):
    vocab = VB * VBLOCKS
    dp = lax.axis_size("dp")
    width = hidden.shape[1]
    chunk = width // dp
    d = lax.axis_index("dp")
    core = d % 2
    zpos = d // 2
    rings = dp // 2
    block_ids = jnp.arange(VBLOCKS, dtype=jnp.int32)
    listed = jnp.any(block_lists[:, :, None] == block_ids[None, None, :], axis=1)
    mask = jnp.repeat(jnp.repeat(listed, TB, axis=0), VB, axis=1).astype(jnp.float32)
    full_head = lax.all_gather(head, "fsdp", axis=0, tiled=True)
    logits = lax.dot_general(
        hidden, full_head, (((1,), (1,)), ((), ())), preferred_element_type=jnp.float32
    )
    columns = jnp.arange(vocab, dtype=jnp.int32)
    hits = (labels[:, None] == columns[None, :]).astype(jnp.float32)
    grad_logits = (
        cotangent[:, None] * (mask * jnp.exp(logits - lse[:, None]) - hits)
    ).astype(jnp.bfloat16)
    def columns_of(parity):
        picks = [
            lax.dynamic_slice_in_dim(hidden, (2 * j + parity) * chunk, chunk, axis=1)
            for j in range(rings)
        ]
        return jnp.concatenate(picks, axis=1)

    contract = (((0,), (0,)), ((), ()))
    send = lax.dot_general(
        grad_logits, columns_of(1 - core), contract, preferred_element_type=jnp.float32
    )
    got = lax.ppermute(send, "dp", [(i, i ^ 1) for i in range(dp)])
    keep = lax.dot_general(
        grad_logits, columns_of(core), contract, preferred_element_type=jnp.float32
    )
    grad_hidden = jnp.dot(grad_logits, full_head, preferred_element_type=jnp.float32)
    keep, grad_hidden = lax.optimization_barrier((keep, grad_hidden))
    chip = keep + got
    part = lax.psum_scatter(chip, "fsdp", scatter_dimension=0, tiled=True)
    def piece(k):
        return lax.dynamic_slice_in_dim(part, (k % rings) * chunk, chunk, axis=1)

    right = [(i, (i + 2) % dp) for i in range(dp)]
    left = [(i, (i - 2) % dp) for i in range(dp)]
    if rings == 4:
        from_left = lax.ppermute(piece(zpos + 2), "dp", right)
        from_right = lax.ppermute(piece(zpos - 1), "dp", left)
        relayed = lax.ppermute(piece(zpos + 1) + from_left, "dp", right)
        acc = piece(zpos) + from_right + relayed
    else:
        acc = piece(zpos - 1)
        for step in range(rings - 1):
            acc = lax.ppermute(acc, "dp", right) + piece(zpos - 2 - step)
    return (grad_hidden.astype(jnp.bfloat16), acc.astype(jnp.bfloat16))


def solution(mesh):
    return jax.shard_map(
        on_device,
        mesh=mesh,
        in_specs=(
            P(("dp", "fsdp"), None),
            P("fsdp", None),
            P(("dp", "fsdp")),
            P(("dp", "fsdp")),
            P(("dp", "fsdp")),
            P(("dp", "fsdp"), None),
        ),
        out_specs=(P(("dp", "fsdp"), None), P("fsdp", "dp")),
        check_vma=False,
    )
```

```python
import jax
import jax.numpy as jnp
from jax import lax
from jax.sharding import PartitionSpec as P

VB = 128
TB = 128
VBLOCKS = 4


def on_device(hidden, head, labels, lse, cotangent, block_lists):
    vocab = VB * VBLOCKS
    dp = lax.axis_size("dp")
    width = hidden.shape[1]
    chunk = width // dp
    d = lax.axis_index("dp")
    core = d % 2
    zpos = d // 2
    rings = dp // 2
    block_ids = jnp.arange(VBLOCKS, dtype=jnp.int32)
    listed = jnp.any(block_lists[:, :, None] == block_ids[None, None, :], axis=1)
    mask = jnp.repeat(jnp.repeat(listed, TB, axis=0), VB, axis=1).astype(jnp.float32)
    full_head = lax.all_gather(head, "fsdp", axis=0, tiled=True)
    logits = lax.dot_general(
        hidden, full_head, (((1,), (1,)), ((), ())), preferred_element_type=jnp.float32
    )
    columns = jnp.arange(vocab, dtype=jnp.int32)
    hits = (labels[:, None] == columns[None, :]).astype(jnp.float32)
    grad_logits = (
        cotangent[:, None] * (mask * jnp.exp(logits - lse[:, None]) - hits)
    ).astype(jnp.bfloat16)
    def columns_of(parity):
        picks = [
            lax.dynamic_slice_in_dim(hidden, (2 * j + parity) * chunk, chunk, axis=1)
            for j in range(rings)
        ]
        return jnp.concatenate(picks, axis=1)

    contract = (((0,), (0,)), ((), ()))
    send = lax.dot_general(
        grad_logits, columns_of(1 - core), contract, preferred_element_type=jnp.float32
    )
    got = lax.ppermute(send, "dp", [(i, i ^ 1) for i in range(dp)])
    grad_hidden = jnp.dot(grad_logits, full_head, preferred_element_type=jnp.float32)
    got, grad_hidden, late_logits = lax.optimization_barrier((got, grad_hidden, grad_logits))
    keep = lax.dot_general(
        late_logits, columns_of(core), contract, preferred_element_type=jnp.float32
    )
    chip = keep + got
    part = lax.psum_scatter(chip, "fsdp", scatter_dimension=0, tiled=True)
    def piece(k):
        return lax.dynamic_slice_in_dim(part, (k % rings) * chunk, chunk, axis=1)

    right = [(i, (i + 2) % dp) for i in range(dp)]
    left = [(i, (i - 2) % dp) for i in range(dp)]
    if rings == 4:
        from_left = lax.ppermute(piece(zpos + 2), "dp", right)
        from_right = lax.ppermute(piece(zpos - 1), "dp", left)
        relayed = lax.ppermute(piece(zpos + 1) + from_left, "dp", right)
        acc = piece(zpos) + from_right + relayed
    else:
        acc = piece(zpos - 1)
        for step in range(rings - 1):
            acc = lax.ppermute(acc, "dp", right) + piece(zpos - 2 - step)
    return (grad_hidden.astype(jnp.bfloat16), acc.astype(jnp.bfloat16))


def solution(mesh):
    return jax.shard_map(
        on_device,
        mesh=mesh,
        in_specs=(
            P(("dp", "fsdp"), None),
            P("fsdp", None),
            P(("dp", "fsdp")),
            P(("dp", "fsdp")),
            P(("dp", "fsdp")),
            P(("dp", "fsdp"), None),
        ),
        out_specs=(P(("dp", "fsdp"), None), P("fsdp", "dp")),
        check_vma=False,
    )
```

```python
import jax
import jax.numpy as jnp
from jax import lax
from jax.sharding import PartitionSpec as P

VB = 128
TB = 128
VBLOCKS = 4


def on_device(hidden, head, labels, lse, cotangent, block_lists):
    vocab = VB * VBLOCKS
    dp = lax.axis_size("dp")
    width = hidden.shape[1]
    chunk = width // dp
    d = lax.axis_index("dp")
    core = d % 2
    zpos = d // 2
    rings = dp // 2
    block_ids = jnp.arange(VBLOCKS, dtype=jnp.int32)
    listed = jnp.any(block_lists[:, :, None] == block_ids[None, None, :], axis=1)
    mask = jnp.repeat(jnp.repeat(listed, TB, axis=0), VB, axis=1).astype(jnp.float32)
    full_head = lax.all_gather(head, "fsdp", axis=0, tiled=True)
    logits = lax.dot_general(
        hidden, full_head, (((1,), (1,)), ((), ())), preferred_element_type=jnp.float32
    )
    columns = jnp.arange(vocab, dtype=jnp.int32)
    hits = (labels[:, None] == columns[None, :]).astype(jnp.float32)
    grad_logits = (
        cotangent[:, None] * (mask * jnp.exp(logits - lse[:, None]) - hits)
    ).astype(jnp.bfloat16)
    def columns_of(parity):
        picks = [
            lax.dynamic_slice_in_dim(hidden, (2 * j + parity) * chunk, chunk, axis=1)
            for j in range(rings)
        ]
        return jnp.concatenate(picks, axis=1)

    contract = (((0,), (0,)), ((), ()))
    send = lax.dot_general(
        grad_logits, columns_of(1 - core), contract, preferred_element_type=jnp.float32
    )
    got = lax.ppermute(send, "dp", [(i, i ^ 1) for i in range(dp)])
    grad_hidden = jnp.dot(grad_logits, full_head, preferred_element_type=jnp.float32)
    got, grad_hidden, late_logits = lax.optimization_barrier((got, grad_hidden, grad_logits))
    keep = lax.dot_general(
        late_logits, columns_of(core), contract, preferred_element_type=jnp.float32
    )
    chip = keep + got
    if lax.axis_size("fsdp") == 16:
        part = plane_scatter(chip)
    else:
        part = lax.psum_scatter(chip, "fsdp", scatter_dimension=0, tiled=True)
    def piece(k):
        return lax.dynamic_slice_in_dim(part, (k % rings) * chunk, chunk, axis=1)

    right = [(i, (i + 2) % dp) for i in range(dp)]
    left = [(i, (i - 2) % dp) for i in range(dp)]
    if rings == 4:
        from_left = lax.ppermute(piece(zpos + 2), "dp", right)
        from_right = lax.ppermute(piece(zpos - 1), "dp", left)
        relayed = lax.ppermute(piece(zpos + 1) + from_left, "dp", right)
        acc = piece(zpos) + from_right + relayed
    else:
        acc = piece(zpos - 1)
        for step in range(rings - 1):
            acc = lax.ppermute(acc, "dp", right) + piece(zpos - 2 - step)
    return (grad_hidden.astype(jnp.bfloat16), acc.astype(jnp.bfloat16))


def ring_scatter(blocks, pos, ahead, behind):
    from_behind = lax.ppermute(blocks(pos + 2), "fsdp", ahead)
    from_ahead = lax.ppermute(blocks(pos - 1), "fsdp", behind)
    relayed = lax.ppermute(blocks(pos + 1) + from_behind, "fsdp", ahead)
    return blocks(pos) + from_ahead + relayed


def mirrored_scatter(blocks, pos, ahead, behind):
    return ring_scatter(lambda k: blocks(-k), -pos, behind, ahead)


def plane_scatter(chip):
    f = lax.axis_index("fsdp")
    xi, yi = f // 4, f % 4
    x_up = [(i, (i + 4) % 16) for i in range(16)]
    x_down = [(i, (i - 4) % 16) for i in range(16)]
    y_up = [(i, 4 * (i // 4) + (i + 1) % 4) for i in range(16)]
    y_down = [(i, 4 * (i // 4) + (i - 1) % 4) for i in range(16)]
    rows, width = chip.shape
    quarter = width // 4
    grid = chip.reshape(4, 4, rows // 16, width)
    outs = []
    for q in range(4):
        data = grid[:, :, :, q * quarter:(q + 1) * quarter]
        scatter = ring_scatter if q % 2 == 0 else mirrored_scatter
        if q < 2:
            first = scatter(lambda k: lax.dynamic_index_in_dim(data, k % 4, 0, False), xi, x_up, x_down)
            done = scatter(lambda k: lax.dynamic_index_in_dim(first, k % 4, 0, False), yi, y_up, y_down)
        else:
            first = scatter(lambda k: lax.dynamic_index_in_dim(data, k % 4, 1, False), yi, y_up, y_down)
            done = scatter(lambda k: lax.dynamic_index_in_dim(first, k % 4, 0, False), xi, x_up, x_down)
        outs.append(done)
    return jnp.concatenate(outs, axis=1)


def solution(mesh):
    return jax.shard_map(
        on_device,
        mesh=mesh,
        in_specs=(
            P(("dp", "fsdp"), None),
            P("fsdp", None),
            P(("dp", "fsdp")),
            P(("dp", "fsdp")),
            P(("dp", "fsdp")),
            P(("dp", "fsdp"), None),
        ),
        out_specs=(P(("dp", "fsdp"), None), P("fsdp", "dp")),
        check_vma=False,
    )
```

```python
import jax
import jax.numpy as jnp
from jax import lax
from jax.sharding import PartitionSpec as P


VB = 128
TB = 128
VBLOCKS = 4


def on_device(hidden, head, labels, lse, cotangent, block_lists):
    vocab = VB * VBLOCKS
    dp = lax.axis_size("dp")
    width = hidden.shape[1]
    chunk = width // dp
    d = lax.axis_index("dp")
    core = d % 2
    zpos = d // 2
    rings = dp // 2
    block_ids = jnp.arange(VBLOCKS, dtype=jnp.int32)
    listed = jnp.any(block_lists[:, :, None] == block_ids[None, None, :], axis=1)
    mask = jnp.repeat(jnp.repeat(listed, TB, axis=0), VB, axis=1).astype(jnp.float32)
    full_head = lax.all_gather(head, "fsdp", axis=0, tiled=True)
    logits = lax.dot_general(
        hidden, full_head, (((1,), (1,)), ((), ())), preferred_element_type=jnp.float32
    )
    columns = jnp.arange(vocab, dtype=jnp.int32)
    hits = (labels[:, None] == columns[None, :]).astype(jnp.float32)
    grad_logits = (
        cotangent[:, None] * (mask * jnp.exp(logits - lse[:, None]) - hits)
    ).astype(jnp.bfloat16)
    def columns_of(parity):
        picks = [
            lax.dynamic_slice_in_dim(hidden, (2 * j + parity) * chunk, chunk, axis=1)
            for j in range(rings)
        ]
        return jnp.concatenate(picks, axis=1)

    contract = (((0,), (0,)), ((), ()))
    send_rows = columns_of(1 - core)
    keep_rows = columns_of(core)
    span = send_rows.shape[1] // 2
    gots = []
    for h in range(2):
        send = lax.dot_general(
            grad_logits, send_rows[:, h * span:(h + 1) * span], contract,
            preferred_element_type=jnp.float32,
        )
        gots.append(lax.ppermute(send, "dp", [(i, i ^ 1) for i in range(dp)]))
    grad_hidden = jnp.dot(grad_logits, full_head, preferred_element_type=jnp.float32)
    gots, grad_hidden, late_logits = lax.optimization_barrier((gots, grad_hidden, grad_logits))
    chips = [
        lax.dot_general(
            late_logits, keep_rows[:, h * span:(h + 1) * span], contract,
            preferred_element_type=jnp.float32,
        )
        + gots[h]
        for h in range(2)
    ]
    chip = jnp.concatenate(chips, axis=1)
    if lax.axis_size("fsdp") == 16:
        part = plane_scatter(chip)
    else:
        part = lax.psum_scatter(chip, "fsdp", scatter_dimension=0, tiled=True)
    def piece(k):
        return lax.dynamic_slice_in_dim(part, (k % rings) * chunk, chunk, axis=1)

    right = [(i, (i + 2) % dp) for i in range(dp)]
    left = [(i, (i - 2) % dp) for i in range(dp)]
    if rings == 4:
        from_left = lax.ppermute(piece(zpos + 2), "dp", right)
        from_right = lax.ppermute(piece(zpos - 1), "dp", left)
        relayed = lax.ppermute(piece(zpos + 1) + from_left, "dp", right)
        acc = piece(zpos) + from_right + relayed
    else:
        acc = piece(zpos - 1)
        for step in range(rings - 1):
            acc = lax.ppermute(acc, "dp", right) + piece(zpos - 2 - step)
    return (grad_hidden.astype(jnp.bfloat16), acc.astype(jnp.bfloat16))


def ring_scatter(blocks, pos, ahead, behind):
    from_behind = lax.ppermute(blocks(pos + 2), "fsdp", ahead)
    from_ahead = lax.ppermute(blocks(pos - 1), "fsdp", behind)
    relayed = lax.ppermute(blocks(pos + 1) + from_behind, "fsdp", ahead)
    return blocks(pos) + from_ahead + relayed


def mirrored_scatter(blocks, pos, ahead, behind):
    return ring_scatter(lambda k: blocks(-k), -pos, behind, ahead)


def plane_scatter(chip):
    f = lax.axis_index("fsdp")
    xi, yi = f // 4, f % 4
    x_up = [(i, (i + 4) % 16) for i in range(16)]
    x_down = [(i, (i - 4) % 16) for i in range(16)]
    y_up = [(i, 4 * (i // 4) + (i + 1) % 4) for i in range(16)]
    y_down = [(i, 4 * (i // 4) + (i - 1) % 4) for i in range(16)]
    rows, width = chip.shape
    quarter = width // 4
    grid = chip.reshape(4, 4, rows // 16, width)
    outs = []
    for q in range(4):
        data = grid[:, :, :, q * quarter:(q + 1) * quarter]
        scatter = ring_scatter if q % 2 == 0 else mirrored_scatter
        if q < 2:
            first = scatter(lambda k: lax.dynamic_index_in_dim(data, k % 4, 0, False), xi, x_up, x_down)
            done = scatter(lambda k: lax.dynamic_index_in_dim(first, k % 4, 0, False), yi, y_up, y_down)
        else:
            first = scatter(lambda k: lax.dynamic_index_in_dim(data, k % 4, 1, False), yi, y_up, y_down)
            done = scatter(lambda k: lax.dynamic_index_in_dim(first, k % 4, 0, False), xi, x_up, x_down)
        outs.append(done)
    return jnp.concatenate(outs, axis=1)


def solution(mesh):
    return jax.shard_map(
        on_device,
        mesh=mesh,
        in_specs=(
            P(("dp", "fsdp"), None),
            P("fsdp", None),
            P(("dp", "fsdp")),
            P(("dp", "fsdp")),
            P(("dp", "fsdp")),
            P(("dp", "fsdp"), None),
        ),
        out_specs=(P(("dp", "fsdp"), None), P("fsdp", "dp")),
        check_vma=False,
    )
```
